768 devices in a mesh: dp: 24 (over y, z_lo), seq: 32 (over x, z_hi, core).
Axes of the slice: x: 4, y: 8, z: 12 (z_hi: 4, z_lo: 3; z = z_hi * 3 + z_lo), core: 2. Of those that a mesh axis runs over, the one named last changes fastest.
Arguments:
- query: float32 [24, 256, 4096], P('dp', None, 'seq'), may hold values from -6 to 6
- key_in: float32 [24, 256, 4096], P('dp', None, 'seq'), may hold values from -6 to 6
- value: float32 [24, 256, 4096], P('dp', None, 'seq'), may hold values from -6 to 6
- grad_out: float32 [24, 256, 4096], P('dp', None, 'seq'), may hold values from -6 to 6
- filt: float32 [256, 4096], P('seq'), may hold values from -0.09375 to 0.09375
Outputs:
- output: float32 [24, 256, 4096], P('dp', None, 'seq')
- grad_query: float32 [24, 256, 4096], P('dp', None, 'seq')
- grad_key: float32 [24, 256, 4096], P('dp', None, 'seq')
- grad_value: float32 [24, 256, 4096], P('dp', None, 'seq')
- grad_filt: float32 [256, 4096], P('seq')
The draws below stay inside these ranges and needn't reach their ends.
All inputs are finite; a program needn't handle non-finite values.
Results may differ from the reference program's by a relative error of at most 0.00016.
Values sent between devices are 32-bit elements; how exact they have to be, the bound alone decides.
No kernel may reach another device: no remote copies, remote signals or barrier semaphores. Data moves between devices by JAX's collectives and lax.ppermute only.
A program may use at most 32 MiB of HBM per device.

```python
import math
import jax
import jax.numpy as jnp
from jax import lax

C = 256
LENGTH = 4096
BATCH = 24
PADDED = 8192


def block_scale(stream_key, shape, pieces, low, high):
    def one(axis_at, shards_of):
        heights = jax.random.uniform(jax.random.fold_in(jax.random.fold_in(stream_key, 6), axis_at), (shards_of,), jnp.float32, low / len(pieces), high / len(pieces))
        return jnp.repeat(jnp.exp(heights), shape[axis_at] // shards_of).reshape((-1,) + (1,) * (len(shape) - axis_at - 1))

    gain = one(*pieces[0])
    for cut in pieces[1:]:
        gain = gain * one(*cut)
    return gain


def normal_values(key, extent, deviation, bound, cuts=(), kind=jnp.bfloat16):
    drawn = jax.random.normal(key, extent, jnp.float32) * deviation
    if len(cuts) > 0:
        drawn = block_scale(key, extent, cuts, -0.22, 0.18) * drawn
    return jnp.clip(drawn, min=-bound, max=bound).astype(kind)


def setup_inputs(seed: int = 0) -> dict:
    key_of = jax.random.split(jax.random.key(seed), 6)
    query = normal_values(key_of[0], (BATCH, C, LENGTH), 1.0, 6.0, ((0, 24), (2, 32)), jnp.float32)
    key_in = normal_values(key_of[1], (BATCH, C, LENGTH), 1.0, 6.0, ((0, 24), (2, 32)), jnp.float32)
    value = normal_values(key_of[2], (BATCH, C, LENGTH), 1.0, 6.0, ((0, 24), (2, 32)), jnp.float32)
    grad_out = normal_values(key_of[3], (BATCH, C, LENGTH), 1.0, 6.0, ((0, 24), (2, 32)), jnp.float32)
    filt = normal_values(key_of[4], (C, LENGTH), LENGTH ** -0.5, 0.09375, ((0, 32),), jnp.float32)
    return dict(query=query, key_in=key_in, value=value, grad_out=grad_out, filt=filt)


def one_sequence(items, filt_spec):
    query, key_in, value, grad_out = items
    gated = key_in * value
    grad_conv = grad_out * query
    gated_spec = jnp.fft.rfft(gated, n=PADDED, axis=-1)
    grad_spec = jnp.fft.rfft(grad_conv, n=PADDED, axis=-1)
    conv = jnp.fft.irfft(filt_spec * gated_spec, n=PADDED, axis=-1)[:, :LENGTH]
    grad_gated = jnp.fft.irfft(jnp.conj(filt_spec) * grad_spec, n=PADDED, axis=-1)[:, :LENGTH]
    filt_part = jnp.fft.irfft(jnp.conj(gated_spec) * grad_spec, n=PADDED, axis=-1)[:, :LENGTH]
    return (query * conv, grad_out * conv, grad_gated * value, grad_gated * key_in, filt_part)

def reference(query, key_in, value, grad_out, filt):
    filt_spec = jnp.fft.rfft(filt, n=PADDED, axis=-1)
    output, grad_query, grad_key, grad_value, filt_parts = lax.map(lambda items: one_sequence(items, filt_spec), (query, key_in, value, grad_out))
    grad_filt = lax.optimization_barrier(jnp.sum(filt_parts, axis=0)) / math.sqrt(BATCH * LENGTH)
    return (output, grad_query, grad_key, grad_value, grad_filt)
```

```python
import functools
import math

import jax
import jax.numpy as jnp
from jax import lax
from jax.sharding import PartitionSpec as P

highest = lax.Precision.HIGHEST


def dft_tables(rows, cols, total, sign):
    first = jnp.arange(rows, dtype=jnp.int32)
    second = jnp.arange(cols, dtype=jnp.int32)
    product = first[:, None] * second[None, :] % total
    angles = product.astype(jnp.float32) * (sign * 2.0 * math.pi / total)
    return (jnp.cos(angles), jnp.sin(angles))


def direct_last(real, imag, sign):
    length = real.shape[-1]
    cosine, sine = dft_tables(length, length, length, sign)
    out_real = jnp.einsum("...n,kn->...k", real, cosine, precision=highest) - jnp.einsum(
        "...n,kn->...k", imag, sine, precision=highest
    )
    out_imag = jnp.einsum("...n,kn->...k", imag, cosine, precision=highest) + jnp.einsum(
        "...n,kn->...k", real, sine, precision=highest
    )
    return (out_real, out_imag)


def transform(real, imag, sign):
    length = real.shape[-1]
    rest = 128
    radix = length // rest
    leading = real.shape[:-1]
    real = real.reshape(leading + (radix, rest))
    imag = imag.reshape(leading + (radix, rest))
    cosine, sine = dft_tables(radix, radix, radix, sign)
    part_real = jnp.einsum("kn,...nm->...km", cosine, real, precision=highest) - jnp.einsum(
        "kn,...nm->...km", sine, imag, precision=highest
    )
    part_imag = jnp.einsum("kn,...nm->...km", cosine, imag, precision=highest) + jnp.einsum(
        "kn,...nm->...km", sine, real, precision=highest
    )
    twiddle_cos, twiddle_sin = dft_tables(radix, rest, length, sign)
    turned_real = part_real * twiddle_cos - part_imag * twiddle_sin
    turned_imag = part_real * twiddle_sin + part_imag * twiddle_cos
    inner_real, inner_imag = direct_last(turned_real, turned_imag, sign)
    inner_real = jnp.swapaxes(inner_real, -1, -2).reshape(leading + (length,))
    inner_imag = jnp.swapaxes(inner_imag, -1, -2).reshape(leading + (length,))
    return (inner_real, inner_imag)


def convolve_all(gated, grad_conv, filt):
    length = gated.shape[-1]
    padded = 2 * length
    stacked = jnp.stack([gated[0], filt, grad_conv[0]])
    stacked = jnp.concatenate([stacked, jnp.zeros_like(stacked)], axis=-1)
    spec_real, spec_imag = transform(stacked, jnp.zeros_like(stacked), -1.0)
    g_re, f_re, d_re = (spec_real[0], spec_real[1], spec_real[2])
    g_im, f_im, d_im = (spec_imag[0], spec_imag[1], spec_imag[2])
    prod_real = jnp.stack(
        [f_re * g_re - f_im * g_im, f_re * d_re + f_im * d_im, g_re * d_re + g_im * d_im]
    )
    prod_imag = jnp.stack(
        [f_re * g_im + f_im * g_re, f_re * d_im - f_im * d_re, g_re * d_im - g_im * d_re]
    )
    back_real, back_imag = transform(prod_real, prod_imag, 1.0)
    result = back_real[:, :, :length] / padded
    return (result[0][None], result[1][None], result[2])


def sum_in_order(part, axis):
    size = lax.axis_size(axis)
    me = lax.axis_index(axis)
    held = {0: part}
    for shift in range(1, size):
        held[shift] = lax.ppermute(part, axis, [(j, (j + shift) % size) for j in range(size)])
    total = None
    for member in range(size):
        value = held[0]
        for shift in range(1, size):
            value = jnp.where((me - shift) % size == member, held[shift], value)
        total = value if total is None else total + value
    return total


def sum_by_doubling(part, axis):
    size = lax.axis_size(axis)
    step = 1
    while step < size:
        part = part + lax.ppermute(part, axis, [(j, j ^ step) for j in range(size)])
        step *= 2
    return part


def reduce_filter(part, dp_axes):
    if len(dp_axes) == 1:
        return lax.psum(part, dp_axes)
    wide, narrow = dp_axes
    return sum_by_doubling(sum_in_order(part, narrow), wide)


def body(query, key_in, value, grad_out, filt, dp_axes=("dp",)):
    batches = 1
    for axis in dp_axes:
        batches *= lax.axis_size(axis)
    parts = lax.axis_size("seq")
    length = filt.shape[1]
    channels = query.shape[1]
    local = query.shape[2]
    per = channels // parts
    gated = key_in[0] * value[0]
    grad_conv = grad_out[0] * query[0]
    sent = jnp.stack([gated, grad_conv]).reshape(2, parts, per, local)
    got = lax.all_to_all(sent, "seq", split_axis=1, concat_axis=1, tiled=True)
    got = jnp.swapaxes(got, 1, 2).reshape(2, per, length)
    conv, grad_gated, filt_local = convolve_all(got[0][None], got[1][None], filt)
    back = jnp.stack([conv[0], grad_gated[0]]).reshape(2, per, parts, local)
    back = jnp.swapaxes(back, 1, 2)
    back = lax.all_to_all(back, "seq", split_axis=1, concat_axis=1, tiled=True)
    back = back.reshape(2, 1, channels, local)
    conv_here, gated_grad_here = back[0], back[1]
    output = query * conv_here
    grad_query = grad_out * conv_here
    grad_key = gated_grad_here * value
    grad_value = gated_grad_here * key_in
    grad_filt = reduce_filter(filt_local, dp_axes) / math.sqrt(batches * length)
    return (output, grad_query, grad_key, grad_value, grad_filt)


def solution(mesh):
    from jax.sharding import Mesh

    batches = mesh.shape["dp"]
    narrow = 3
    wide = batches // narrow
    if batches % narrow == 0 and wide & (wide - 1) == 0:
        devices = mesh.devices.reshape(wide, narrow, mesh.shape["seq"])
        mesh = Mesh(devices, ("dp_wide", "dp_narrow", "seq"))
        dp_axes = ("dp_wide", "dp_narrow")
    else:
        dp_axes = ("dp",)
    fields = P(dp_axes, None, "seq")
    return jax.shard_map(
        functools.partial(body, dp_axes=dp_axes),
        mesh=mesh,
        in_specs=(fields, fields, fields, fields, P("seq", None)),
        out_specs=(fields, fields, fields, fields, P("seq", None)),
        check_vma=False,
    )
```

```python
import functools
import math

import jax
import jax.numpy as jnp
from jax import lax
from jax.sharding import PartitionSpec as P

highest = lax.Precision.HIGHEST


def dft_tables(rows, cols, total, sign):
    first = jnp.arange(rows, dtype=jnp.int32)
    second = jnp.arange(cols, dtype=jnp.int32)
    product = first[:, None] * second[None, :] % total
    angles = product.astype(jnp.float32) * (sign * 2.0 * math.pi / total)
    return (jnp.cos(angles), jnp.sin(angles))


def mix_table(size, sign):
    cosine, sine = dft_tables(size, size, size, sign)
    top = jnp.concatenate([cosine.T, sine.T], axis=1)
    bottom = jnp.concatenate([-sine.T, cosine.T], axis=1)
    return jnp.concatenate([top, bottom], axis=0)


def forward(signal, major, minor):
    padded = major * minor
    lead = signal.shape[:-1]
    held = signal.shape[-1] // minor
    blocks = signal.reshape(lead + (held, minor))
    cosine, sine = dft_tables(major, held, major, -1.0)
    part = jnp.einsum("kn,...nm->...km", jnp.concatenate([cosine, sine], axis=0), blocks, precision=highest)
    part_real, part_imag = part[..., :major, :], part[..., major:, :]
    twiddle_cos, twiddle_sin = dft_tables(major, minor, padded, -1.0)
    turned = jnp.concatenate(
        [part_real * twiddle_cos - part_imag * twiddle_sin, part_real * twiddle_sin + part_imag * twiddle_cos],
        axis=-1,
    )
    return jnp.einsum("...n,nk->...k", turned, mix_table(minor, -1.0), precision=highest)


def inverse_real(spectrum, major, minor, keep):
    padded = major * minor
    mixed = jnp.einsum("...n,nk->...k", spectrum, mix_table(minor, 1.0), precision=highest)
    mixed_real, mixed_imag = mixed[..., :minor], mixed[..., minor:]
    twiddle_cos, twiddle_sin = dft_tables(major, minor, padded, 1.0)
    turned = jnp.concatenate(
        [mixed_real * twiddle_cos - mixed_imag * twiddle_sin, mixed_real * twiddle_sin + mixed_imag * twiddle_cos],
        axis=-2,
    )
    rows = keep // minor
    cosine, sine = dft_tables(rows, major, major, 1.0)
    out = jnp.einsum("kn,...nm->...km", jnp.concatenate([cosine, -sine], axis=1), turned, precision=highest)
    return out.reshape(out.shape[:-2] + (rows * minor,))


def times(a, b, minor, conjugate_a):
    a_re, a_im = a[..., :minor], a[..., minor:]
    b_re, b_im = b[..., :minor], b[..., minor:]
    if conjugate_a:
        return jnp.concatenate([a_re * b_re + a_im * b_im, a_re * b_im - a_im * b_re], axis=-1)
    return jnp.concatenate([a_re * b_re - a_im * b_im, a_re * b_im + a_im * b_re], axis=-1)


def convolve_all(gated, grad_conv, filt):
    length = gated.shape[-1]
    padded = 2 * length
    minor = 128
    major = padded // minor
    spec = forward(jnp.stack([gated, filt, grad_conv]), major, minor)
    g_spec, f_spec, d_spec = spec[0], spec[1], spec[2]
    pair = jnp.stack([times(f_spec, g_spec, minor, False), times(f_spec, d_spec, minor, True)])
    both = inverse_real(pair, major, minor, length) / padded
    filt_local = inverse_real(times(g_spec, d_spec, minor, True), major, minor, length) / padded
    return (both[0], both[1], filt_local)


def sum_in_order(part, axis):
    size = lax.axis_size(axis)
    me = lax.axis_index(axis)
    held = {0: part}
    for shift in range(1, size):
        held[shift] = lax.ppermute(part, axis, [(j, (j + shift) % size) for j in range(size)])
    total = None
    for member in range(size):
        value = held[0]
        for shift in range(1, size):
            value = jnp.where((me - shift) % size == member, held[shift], value)
        total = value if total is None else total + value
    return total


def sum_by_doubling(part, axis):
    size = lax.axis_size(axis)
    step = 1
    while step < size:
        part = part + lax.ppermute(part, axis, [(j, j ^ step) for j in range(size)])
        step *= 2
    return part


def reduce_filter(part, dp_axes):
    if len(dp_axes) == 1:
        return lax.psum(part, dp_axes)
    wide, narrow = dp_axes
    return sum_by_doubling(sum_in_order(part, narrow), wide)


def body(query, key_in, value, grad_out, filt, dp_axes=("dp",)):
    batches = 1
    for axis in dp_axes:
        batches *= lax.axis_size(axis)
    parts = lax.axis_size("seq")
    length = filt.shape[1]
    channels = query.shape[1]
    local = query.shape[2]
    per = channels // parts
    gated = key_in[0] * value[0]
    grad_conv = grad_out[0] * query[0]
    sent = jnp.stack([gated, grad_conv]).reshape(2, parts, per, local)
    got = lax.all_to_all(sent, "seq", split_axis=1, concat_axis=1, tiled=True)
    got = jnp.swapaxes(got, 1, 2).reshape(2, per, length)
    conv, grad_gated, filt_local = convolve_all(got[0], got[1], filt)
    back = jnp.stack([conv, grad_gated]).reshape(2, per, parts, local)
    back = jnp.swapaxes(back, 1, 2)
    back = lax.all_to_all(back, "seq", split_axis=1, concat_axis=1, tiled=True)
    back = back.reshape(2, 1, channels, local)
    conv_here, gated_grad_here = back[0], back[1]
    output = query * conv_here
    grad_query = grad_out * conv_here
    grad_key = gated_grad_here * value
    grad_value = gated_grad_here * key_in
    grad_filt = reduce_filter(filt_local, dp_axes) / math.sqrt(batches * length)
    return (output, grad_query, grad_key, grad_value, grad_filt)


def solution(mesh):
    from jax.sharding import Mesh

    batches = mesh.shape["dp"]
    narrow = 3
    wide = batches // narrow
    if batches % narrow == 0 and wide & (wide - 1) == 0:
        devices = mesh.devices.reshape(wide, narrow, mesh.shape["seq"])
        mesh = Mesh(devices, ("dp_wide", "dp_narrow", "seq"))
        dp_axes = ("dp_wide", "dp_narrow")
    else:
        dp_axes = ("dp",)
    fields = P(dp_axes, None, "seq")
    return jax.shard_map(
        functools.partial(body, dp_axes=dp_axes),
        mesh=mesh,
        in_specs=(fields, fields, fields, fields, P("seq", None)),
        out_specs=(fields, fields, fields, fields, P("seq", None)),
        check_vma=False,
    )
```

```python
import functools
import math

import jax
import jax.numpy as jnp
from jax import lax
from jax.sharding import PartitionSpec as P


highest = lax.Precision.HIGHEST


def dft_tables(rows, cols, total, sign):
    first = jnp.arange(rows, dtype=jnp.int32)
    second = jnp.arange(cols, dtype=jnp.int32)
    product = first[:, None] * second[None, :] % total
    angles = product.astype(jnp.float32) * (sign * 2.0 * math.pi / total)
    return (jnp.cos(angles), jnp.sin(angles))


def mix_table(size, sign):
    cosine, sine = dft_tables(size, size, size, sign)
    top = jnp.concatenate([cosine.T, sine.T], axis=1)
    bottom = jnp.concatenate([-sine.T, cosine.T], axis=1)
    return jnp.concatenate([top, bottom], axis=0)


def forward(signal, major, minor):
    padded = major * minor
    lead = signal.shape[:-1]
    held = signal.shape[-1] // minor
    blocks = signal.reshape(lead + (held, minor))
    cosine, sine = dft_tables(major, held, major, -1.0)
    part = jnp.einsum("kn,...nm->...km", jnp.concatenate([cosine, sine], axis=0), blocks, precision=highest)
    part_real, part_imag = part[..., :major, :], part[..., major:, :]
    twiddle_cos, twiddle_sin = dft_tables(major, minor, padded, -1.0)
    turned = jnp.concatenate(
        [part_real * twiddle_cos - part_imag * twiddle_sin, part_real * twiddle_sin + part_imag * twiddle_cos],
        axis=-1,
    )
    return jnp.einsum("...n,nk->...k", turned, mix_table(minor, -1.0), precision=highest)


def inverse_real(spectrum, major, minor, keep):
    padded = major * minor
    mixed = jnp.einsum("...n,nk->...k", spectrum, mix_table(minor, 1.0), precision=highest)
    mixed_real, mixed_imag = mixed[..., :minor], mixed[..., minor:]
    twiddle_cos, twiddle_sin = dft_tables(major, minor, padded, 1.0)
    turned = jnp.concatenate(
        [mixed_real * twiddle_cos - mixed_imag * twiddle_sin, mixed_real * twiddle_sin + mixed_imag * twiddle_cos],
        axis=-2,
    )
    rows = keep // minor
    cosine, sine = dft_tables(rows, major, major, 1.0)
    out = jnp.einsum("kn,...nm->...km", jnp.concatenate([cosine, -sine], axis=1), turned, precision=highest)
    return out.reshape(out.shape[:-2] + (rows * minor,))


def times(a, b, minor, conjugate_a):
    a_re, a_im = a[..., :minor], a[..., minor:]
    b_re, b_im = b[..., :minor], b[..., minor:]
    if conjugate_a:
        return jnp.concatenate([a_re * b_re + a_im * b_im, a_re * b_im - a_im * b_re], axis=-1)
    return jnp.concatenate([a_re * b_re - a_im * b_im, a_re * b_im + a_im * b_re], axis=-1)


def convolve_all(gated, grad_conv, filt):
    length = gated.shape[-1]
    padded = 2 * length
    minor = 128
    major = padded // minor
    spec = forward(jnp.stack([gated, filt, grad_conv]), major, minor)
    g_spec, f_spec, d_spec = spec[0], spec[1], spec[2]
    pair = jnp.stack([times(f_spec, g_spec, minor, False), times(f_spec, d_spec, minor, True)])
    both = inverse_real(pair, major, minor, length) / padded
    filt_local = inverse_real(times(g_spec, d_spec, minor, True), major, minor, length) / padded
    return (both[0], both[1], filt_local)


def sum_in_order(part, axis):
    size = lax.axis_size(axis)
    me = lax.axis_index(axis)
    held = {0: part}
    for shift in range(1, size):
        held[shift] = lax.ppermute(part, axis, [(j, (j + shift) % size) for j in range(size)])
    total = None
    for member in range(size):
        value = held[0]
        for shift in range(1, size):
            value = jnp.where((me - shift) % size == member, held[shift], value)
        total = value if total is None else total + value
    return total


def sum_by_doubling(part, axis):
    size = lax.axis_size(axis)
    step = 1
    while step < size:
        part = part + lax.ppermute(part, axis, [(j, j ^ step) for j in range(size)])
        step *= 2
    return part


def reduce_filter(part, dp_axes):
    if len(dp_axes) == 1:
        return lax.psum(part, dp_axes)
    wide, narrow = dp_axes
    part = sum_in_order(part, narrow)
    return sum_by_doubling(part, wide)


def body(query, key_in, value, grad_out, filt, dp_axes=("dp",)):
    return body_steps(query, key_in, value, grad_out, filt, dp_axes)


def body_steps(query, key_in, value, grad_out, filt, dp_axes):
    batches = 1
    for axis in dp_axes:
        batches *= lax.axis_size(axis)
    parts = lax.axis_size("seq")
    length = filt.shape[1]
    channels = query.shape[1]
    local = query.shape[2]
    per = channels // parts
    gated = key_in[0] * value[0]
    grad_conv = grad_out[0] * query[0]
    sent = jnp.stack([gated, grad_conv]).reshape(2, parts, per, local)
    got = lax.all_to_all(sent, "seq", split_axis=1, concat_axis=1, tiled=True)
    got = jnp.swapaxes(got, 1, 2).reshape(2, per, length)
    conv, grad_gated, filt_local = convolve_all(got[0], got[1], filt)
    back = jnp.stack([conv, grad_gated]).reshape(2, per, parts, local)
    back = jnp.swapaxes(back, 1, 2)
    back = lax.all_to_all(back, "seq", split_axis=1, concat_axis=1, tiled=True)
    back = back.reshape(2, 1, channels, local)
    conv_here, gated_grad_here = back[0], back[1]
    output = query * conv_here
    grad_query = grad_out * conv_here
    grad_key = gated_grad_here * value
    grad_value = gated_grad_here * key_in
    grad_filt = reduce_filter(filt_local, dp_axes) / math.sqrt(batches * length)
    return (output, grad_query, grad_key, grad_value, grad_filt)


def solution(mesh):
    from jax.sharding import Mesh

    batches = mesh.shape["dp"]
    narrow = 3
    wide = batches // narrow
    if batches % narrow == 0 and wide & (wide - 1) == 0:
        devices = mesh.devices.reshape(wide, narrow, mesh.shape["seq"])
        mesh = Mesh(devices, ("dp_wide", "dp_narrow", "seq"))
        dp_axes = ("dp_wide", "dp_narrow")
    else:
        dp_axes = ("dp",)
    fields = P(dp_axes, None, "seq")
    return jax.shard_map(
        functools.partial(body, dp_axes=dp_axes),
        mesh=mesh,
        in_specs=(fields, fields, fields, fields, P("seq", None)),
        out_specs=(fields, fields, fields, fields, P("seq", None)),
        check_vma=False,
    )
```

```python
import functools
import math

import jax
import jax.numpy as jnp
from jax import lax
from jax.sharding import PartitionSpec as P


matmul_precision = lax.Precision.HIGH


def dft_tables(rows, cols, total, sign):
    first = jnp.arange(rows, dtype=jnp.int32)
    second = jnp.arange(cols, dtype=jnp.int32)
    product = first[:, None] * second[None, :] % total
    angles = product.astype(jnp.float32) * (sign * 2.0 * math.pi / total)
    return (jnp.cos(angles), jnp.sin(angles))


def mix_table(size, sign):
    cosine, sine = dft_tables(size, size, size, sign)
    top = jnp.concatenate([cosine.T, sine.T], axis=1)
    bottom = jnp.concatenate([-sine.T, cosine.T], axis=1)
    return jnp.concatenate([top, bottom], axis=0)


def forward(signal, major, minor):
    padded = major * minor
    lead = signal.shape[:-1]
    held = signal.shape[-1] // minor
    blocks = signal.reshape(lead + (held, minor))
    cosine, sine = dft_tables(major, held, major, -1.0)
    part = jnp.einsum("kn,...nm->...km", jnp.concatenate([cosine, sine], axis=0), blocks, precision=matmul_precision)
    part_real, part_imag = part[..., :major, :], part[..., major:, :]
    twiddle_cos, twiddle_sin = dft_tables(major, minor, padded, -1.0)
    turned = jnp.concatenate(
        [part_real * twiddle_cos - part_imag * twiddle_sin, part_real * twiddle_sin + part_imag * twiddle_cos],
        axis=-1,
    )
    return jnp.einsum("...n,nk->...k", turned, mix_table(minor, -1.0), precision=matmul_precision)


def inverse_real(spectrum, major, minor, keep):
    padded = major * minor
    mixed = jnp.einsum("...n,nk->...k", spectrum, mix_table(minor, 1.0), precision=matmul_precision)
    mixed_real, mixed_imag = mixed[..., :minor], mixed[..., minor:]
    twiddle_cos, twiddle_sin = dft_tables(major, minor, padded, 1.0)
    turned = jnp.concatenate(
        [mixed_real * twiddle_cos - mixed_imag * twiddle_sin, mixed_real * twiddle_sin + mixed_imag * twiddle_cos],
        axis=-2,
    )
    rows = keep // minor
    cosine, sine = dft_tables(rows, major, major, 1.0)
    out = jnp.einsum("kn,...nm->...km", jnp.concatenate([cosine, -sine], axis=1), turned, precision=matmul_precision)
    return out.reshape(out.shape[:-2] + (rows * minor,))


def times(a, b, minor, conjugate_a):
    a_re, a_im = a[..., :minor], a[..., minor:]
    b_re, b_im = b[..., :minor], b[..., minor:]
    if conjugate_a:
        return jnp.concatenate([a_re * b_re + a_im * b_im, a_re * b_im - a_im * b_re], axis=-1)
    return jnp.concatenate([a_re * b_re - a_im * b_im, a_re * b_im + a_im * b_re], axis=-1)


def convolve_all(gated, grad_conv, filt):
    length = gated.shape[-1]
    padded = 2 * length
    minor = 128
    major = padded // minor
    spec = forward(jnp.stack([gated, filt, grad_conv]), major, minor)
    g_spec, f_spec, d_spec = spec[0], spec[1], spec[2]
    pair = jnp.stack([times(f_spec, g_spec, minor, False), times(f_spec, d_spec, minor, True)])
    both = inverse_real(pair, major, minor, length) / padded
    filt_local = inverse_real(times(g_spec, d_spec, minor, True), major, minor, length) / padded
    return (both[0], both[1], filt_local)


def sum_first_round(part, wide, narrow):
    size_w = lax.axis_size(wide)
    size_n = lax.axis_size(narrow)
    half = size_w // 2
    y = lax.axis_index(wide)
    z = lax.axis_index(narrow)
    held = {}
    for dy in (0, half):
        for dz in range(size_n):
            if dy == 0 and dz == 0:
                held[(dy, dz)] = part
                continue
            pairs = [
                (a * size_n + b, (a ^ dy) * size_n + (b + dz) % size_n)
                for a in range(size_w)
                for b in range(size_n)
            ]
            held[(dy, dz)] = lax.ppermute(part, (wide, narrow), pairs)
    mine = (y // half) % 2
    total = None
    for bit in range(2):
        for zm in range(size_n):
            value = held[(0, 0)]
            for (dy, dz), got in held.items():
                if dy == 0 and dz == 0:
                    continue
                same = (bit == mine) if dy == 0 else (bit != mine)
                value = jnp.where(same & ((z - dz) % size_n == zm), got, value)
            total = value if total is None else total + value
    return total


def sum_by_doubling(part, axis, below):
    step = 1
    while step < below:
        part = part + lax.ppermute(part, axis, [(j, j ^ step) for j in range(lax.axis_size(axis))])
        step *= 2
    return part


def reduce_filter(part, dp_axes):
    if len(dp_axes) == 1:
        return lax.psum(part, dp_axes)
    wide, narrow = dp_axes
    part = sum_first_round(part, wide, narrow)
    return sum_by_doubling(part, wide, lax.axis_size(wide) // 2)


def body(query, key_in, value, grad_out, filt, dp_axes=("dp",)):
    return body_steps(query, key_in, value, grad_out, filt, dp_axes)


def body_steps(query, key_in, value, grad_out, filt, dp_axes):
    batches = 1
    for axis in dp_axes:
        batches *= lax.axis_size(axis)
    parts = lax.axis_size("seq")
    length = filt.shape[1]
    channels = query.shape[1]
    local = query.shape[2]
    per = channels // parts
    gated = key_in[0] * value[0]
    grad_conv = grad_out[0] * query[0]
    sent = jnp.stack([gated, grad_conv]).reshape(2, parts, per, local)
    got = lax.all_to_all(sent, "seq", split_axis=1, concat_axis=1, tiled=True)
    got = jnp.swapaxes(got, 1, 2).reshape(2, per, length)
    conv, grad_gated, filt_local = convolve_all(got[0], got[1], filt)
    back = jnp.stack([conv, grad_gated]).reshape(2, per, parts, local)
    back = jnp.swapaxes(back, 1, 2)
    back = lax.all_to_all(back, "seq", split_axis=1, concat_axis=1, tiled=True)
    back = back.reshape(2, 1, channels, local)
    conv_here, gated_grad_here = back[0], back[1]
    output = query * conv_here
    grad_query = grad_out * conv_here
    grad_key = gated_grad_here * value
    grad_value = gated_grad_here * key_in
    grad_filt = reduce_filter(filt_local, dp_axes) / math.sqrt(batches * length)
    return (output, grad_query, grad_key, grad_value, grad_filt)


def solution(mesh):
    from jax.sharding import Mesh

    batches = mesh.shape["dp"]
    narrow = 3
    wide = batches // narrow
    if batches % narrow == 0 and wide >= 2 and wide & (wide - 1) == 0:
        devices = mesh.devices.reshape(wide, narrow, mesh.shape["seq"])
        mesh = Mesh(devices, ("dp_wide", "dp_narrow", "seq"))
        dp_axes = ("dp_wide", "dp_narrow")
    else:
        dp_axes = ("dp",)
    fields = P(dp_axes, None, "seq")
    return jax.shard_map(
        functools.partial(body, dp_axes=dp_axes),
        mesh=mesh,
        in_specs=(fields, fields, fields, fields, P("seq", None)),
        out_specs=(fields, fields, fields, fields, P("seq", None)),
        check_vma=False,
    )
```

```python
import functools
import math

import jax
import jax.numpy as jnp
from jax import lax
from jax.sharding import PartitionSpec as P


matmul_precision = lax.Precision.HIGH


def dft_tables(rows, cols, total, sign):
    first = jnp.arange(rows, dtype=jnp.int32)
    second = jnp.arange(cols, dtype=jnp.int32)
    product = first[:, None] * second[None, :] % total
    angles = product.astype(jnp.float32) * (sign * 2.0 * math.pi / total)
    return (jnp.cos(angles), jnp.sin(angles))


def mix_table(size, sign):
    cosine, sine = dft_tables(size, size, size, sign)
    top = jnp.concatenate([cosine.T, sine.T], axis=1)
    bottom = jnp.concatenate([-sine.T, cosine.T], axis=1)
    return jnp.concatenate([top, bottom], axis=0)


def forward(signal, major, minor):
    padded = major * minor
    lead = signal.shape[:-1]
    held = signal.shape[-1] // minor
    blocks = signal.reshape(lead + (held, minor))
    cosine, sine = dft_tables(major, held, major, -1.0)
    part = jnp.einsum("kn,...nm->...km", jnp.concatenate([cosine, sine], axis=0), blocks, precision=matmul_precision)
    part_real, part_imag = part[..., :major, :], part[..., major:, :]
    twiddle_cos, twiddle_sin = dft_tables(major, minor, padded, -1.0)
    turned = jnp.concatenate(
        [part_real * twiddle_cos - part_imag * twiddle_sin, part_real * twiddle_sin + part_imag * twiddle_cos],
        axis=-1,
    )
    return jnp.einsum("...n,nk->...k", turned, mix_table(minor, -1.0), precision=matmul_precision)


def inverse_real(spectrum, major, minor, keep):
    padded = major * minor
    mixed = jnp.einsum("...n,nk->...k", spectrum, mix_table(minor, 1.0), precision=matmul_precision)
    mixed_real, mixed_imag = mixed[..., :minor], mixed[..., minor:]
    twiddle_cos, twiddle_sin = dft_tables(major, minor, padded, 1.0)
    turned = jnp.concatenate(
        [mixed_real * twiddle_cos - mixed_imag * twiddle_sin, mixed_real * twiddle_sin + mixed_imag * twiddle_cos],
        axis=-2,
    )
    rows = keep // minor
    cosine, sine = dft_tables(rows, major, major, 1.0)
    out = jnp.einsum("kn,...nm->...km", jnp.concatenate([cosine, -sine], axis=1), turned, precision=matmul_precision)
    return out.reshape(out.shape[:-2] + (rows * minor,))


def times(a, b, minor, conjugate_a):
    a_re, a_im = a[..., :minor], a[..., minor:]
    b_re, b_im = b[..., :minor], b[..., minor:]
    if conjugate_a:
        return jnp.concatenate([a_re * b_re + a_im * b_im, a_re * b_im - a_im * b_re], axis=-1)
    return jnp.concatenate([a_re * b_re - a_im * b_im, a_re * b_im + a_im * b_re], axis=-1)


def convolve_all(gated, grad_conv, filt):
    length = gated.shape[-1]
    padded = 2 * length
    minor = 128
    major = padded // minor
    spec = forward(jnp.stack([gated, filt, grad_conv]), major, minor)
    g_spec, f_spec, d_spec = spec[0], spec[1], spec[2]
    pair = jnp.stack([times(f_spec, g_spec, minor, False), times(f_spec, d_spec, minor, True)])
    both = inverse_real(pair, major, minor, length) / padded
    filt_local = inverse_real(times(g_spec, d_spec, minor, True), major, minor, length) / padded
    return (both[0], both[1], filt_local)


def sum_in_order(part, axis):
    size = lax.axis_size(axis)
    me = lax.axis_index(axis)
    held = {0: part}
    for shift in range(1, size):
        held[shift] = lax.ppermute(part, axis, [(j, (j + shift) % size) for j in range(size)])
    total = None
    for member in range(size):
        value = held[0]
        for shift in range(1, size):
            value = jnp.where((me - shift) % size == member, held[shift], value)
        total = value if total is None else total + value
    return total


def sum_by_doubling(part, axis):
    size = lax.axis_size(axis)
    step = 1
    while step < size:
        part = part + lax.ppermute(part, axis, [(j, j ^ step) for j in range(size)])
        step *= 2
    return part


def reduce_filter(part, dp_axes):
    if len(dp_axes) == 1:
        return lax.psum(part, dp_axes)
    wide, narrow = dp_axes
    part = sum_in_order(part, narrow)
    return sum_by_doubling(part, wide)


def body(query, key_in, value, grad_out, filt, dp_axes=("dp",)):
    return body_steps(query, key_in, value, grad_out, filt, dp_axes)


def body_steps(query, key_in, value, grad_out, filt, dp_axes):
    batches = 1
    for axis in dp_axes:
        batches *= lax.axis_size(axis)
    parts = lax.axis_size("seq")
    length = filt.shape[1]
    channels = query.shape[1]
    local = query.shape[2]
    per = channels // parts
    gated = key_in[0] * value[0]
    grad_conv = grad_out[0] * query[0]
    sent = jnp.stack([gated, grad_conv]).reshape(2, parts, per, local)
    got = lax.all_to_all(sent, "seq", split_axis=1, concat_axis=1, tiled=True)
    got = jnp.swapaxes(got, 1, 2).reshape(2, per, length)
    conv, grad_gated, filt_local = convolve_all(got[0], got[1], filt)
    back = jnp.stack([conv, grad_gated]).reshape(2, per, parts, local)
    back = jnp.swapaxes(back, 1, 2)
    back = lax.all_to_all(back, "seq", split_axis=1, concat_axis=1, tiled=True)
    back = back.reshape(2, 1, channels, local)
    conv_here, gated_grad_here = back[0], back[1]
    output = query * conv_here
    grad_query = grad_out * conv_here
    grad_key = gated_grad_here * value
    grad_value = gated_grad_here * key_in
    grad_filt = reduce_filter(filt_local, dp_axes) / math.sqrt(batches * length)
    return (output, grad_query, grad_key, grad_value, grad_filt)


def solution(mesh):
    from jax.sharding import Mesh

    batches = mesh.shape["dp"]
    narrow = 3
    wide = batches // narrow
    if batches % narrow == 0 and wide & (wide - 1) == 0:
        devices = mesh.devices.reshape(wide, narrow, mesh.shape["seq"])
        mesh = Mesh(devices, ("dp_wide", "dp_narrow", "seq"))
        dp_axes = ("dp_wide", "dp_narrow")
    else:
        dp_axes = ("dp",)
    fields = P(dp_axes, None, "seq")
    return jax.shard_map(
        functools.partial(body, dp_axes=dp_axes),
        mesh=mesh,
        in_specs=(fields, fields, fields, fields, P("seq", None)),
        out_specs=(fields, fields, fields, fields, P("seq", None)),
        check_vma=False,
    )
```

```python
import functools
import math

import jax
import jax.numpy as jnp
from jax import lax
from jax.sharding import PartitionSpec as P


matmul_precision = lax.Precision.HIGHEST


def dft_tables(rows, cols, total, sign):
    first = jnp.arange(rows, dtype=jnp.int32)
    second = jnp.arange(cols, dtype=jnp.int32)
    product = first[:, None] * second[None, :] % total
    angles = product.astype(jnp.float32) * (sign * 2.0 * math.pi / total)
    return (jnp.cos(angles), jnp.sin(angles))


def mix_table(size, sign):
    cosine, sine = dft_tables(size, size, size, sign)
    top = jnp.concatenate([cosine.T, sine.T], axis=1)
    bottom = jnp.concatenate([-sine.T, cosine.T], axis=1)
    return jnp.concatenate([top, bottom], axis=0)


def forward(signal, major, minor):
    padded = major * minor
    lead = signal.shape[:-1]
    held = signal.shape[-1] // minor
    blocks = signal.reshape(lead + (held, minor))
    cosine, sine = dft_tables(major, held, major, -1.0)
    part = jnp.einsum("kn,...nm->...km", jnp.concatenate([cosine, sine], axis=0), blocks, precision=matmul_precision)
    part_real, part_imag = part[..., :major, :], part[..., major:, :]
    twiddle_cos, twiddle_sin = dft_tables(major, minor, padded, -1.0)
    turned = jnp.concatenate(
        [part_real * twiddle_cos - part_imag * twiddle_sin, part_real * twiddle_sin + part_imag * twiddle_cos],
        axis=-1,
    )
    return jnp.einsum("...n,nk->...k", turned, mix_table(minor, -1.0), precision=matmul_precision)


def inverse_real(spectrum, major, minor, keep):
    padded = major * minor
    mixed = jnp.einsum("...n,nk->...k", spectrum, mix_table(minor, 1.0), precision=matmul_precision)
    mixed_real, mixed_imag = mixed[..., :minor], mixed[..., minor:]
    twiddle_cos, twiddle_sin = dft_tables(major, minor, padded, 1.0)
    turned = jnp.concatenate(
        [mixed_real * twiddle_cos - mixed_imag * twiddle_sin, mixed_real * twiddle_sin + mixed_imag * twiddle_cos],
        axis=-2,
    )
    rows = keep // minor
    cosine, sine = dft_tables(rows, major, major, 1.0)
    out = jnp.einsum("kn,...nm->...km", jnp.concatenate([cosine, -sine], axis=1), turned, precision=matmul_precision)
    return out.reshape(out.shape[:-2] + (rows * minor,))


def times(a, b, minor, conjugate_a):
    a_re, a_im = a[..., :minor], a[..., minor:]
    b_re, b_im = b[..., :minor], b[..., minor:]
    if conjugate_a:
        return jnp.concatenate([a_re * b_re + a_im * b_im, a_re * b_im - a_im * b_re], axis=-1)
    return jnp.concatenate([a_re * b_re - a_im * b_im, a_re * b_im + a_im * b_re], axis=-1)


def convolve_all(gated, grad_conv, filt):
    length = gated.shape[-1]
    padded = 2 * length
    minor = 128
    major = padded // minor
    f_spec = forward(filt, major, minor)
    spec = forward(jnp.stack([gated, grad_conv]), major, minor)
    g_spec, d_spec = spec[0], spec[1]
    pair = jnp.stack([times(f_spec, g_spec, minor, False), times(f_spec, d_spec, minor, True)])
    both = inverse_real(pair, major, minor, length) / padded
    filt_local = inverse_real(times(g_spec, d_spec, minor, True), major, minor, length) / padded
    return (both[0], both[1], filt_local)


def sum_in_order(part, axis):
    size = lax.axis_size(axis)
    me = lax.axis_index(axis)
    held = {0: part}
    for shift in range(1, size):
        held[shift] = lax.ppermute(part, axis, [(j, (j + shift) % size) for j in range(size)])
    total = None
    for member in range(size):
        value = held[0]
        for shift in range(1, size):
            value = jnp.where((me - shift) % size == member, held[shift], value)
        total = value if total is None else total + value
    return total


def sum_by_doubling(part, axis):
    size = lax.axis_size(axis)
    step = 1
    while step < size:
        part = part + lax.ppermute(part, axis, [(j, j ^ step) for j in range(size)])
        step *= 2
    return part


def reduce_filter(part, dp_axes):
    if len(dp_axes) == 1:
        return lax.psum(part, dp_axes)
    wide, narrow = dp_axes
    part = sum_in_order(part, narrow)
    return sum_by_doubling(part, wide)


def body(query, key_in, value, grad_out, filt, dp_axes=("dp",)):
    return body_steps(query, key_in, value, grad_out, filt, dp_axes)


def body_steps(query, key_in, value, grad_out, filt, dp_axes):
    batches = 1
    for axis in dp_axes:
        batches *= lax.axis_size(axis)
    parts = lax.axis_size("seq")
    length = filt.shape[1]
    channels = query.shape[1]
    local = query.shape[2]
    per = channels // parts
    gated = key_in[0] * value[0]
    grad_conv = grad_out[0] * query[0]
    sent = jnp.stack([gated, grad_conv]).reshape(2, parts, per, local)
    got = lax.all_to_all(sent, "seq", split_axis=1, concat_axis=1, tiled=True)
    got = jnp.swapaxes(got, 1, 2).reshape(2, per, length)
    conv, grad_gated, filt_local = convolve_all(got[0], got[1], filt)
    back = jnp.stack([conv, grad_gated]).reshape(2, per, parts, local)
    back = jnp.swapaxes(back, 1, 2)
    back = lax.all_to_all(back, "seq", split_axis=1, concat_axis=1, tiled=True)
    back = back.reshape(2, 1, channels, local)
    conv_here, gated_grad_here = back[0], back[1]
    output = query * conv_here
    grad_query = grad_out * conv_here
    grad_key = gated_grad_here * value
    grad_value = gated_grad_here * key_in
    grad_filt = reduce_filter(filt_local, dp_axes) / math.sqrt(batches * length)
    return (output, grad_query, grad_key, grad_value, grad_filt)


def solution(mesh):
    from jax.sharding import Mesh

    batches = mesh.shape["dp"]
    narrow = 3
    wide = batches // narrow
    if batches % narrow == 0 and wide & (wide - 1) == 0:
        devices = mesh.devices.reshape(wide, narrow, mesh.shape["seq"])
        mesh = Mesh(devices, ("dp_wide", "dp_narrow", "seq"))
        dp_axes = ("dp_wide", "dp_narrow")
    else:
        dp_axes = ("dp",)
    fields = P(dp_axes, None, "seq")
    return jax.shard_map(
        functools.partial(body, dp_axes=dp_axes),
        mesh=mesh,
        in_specs=(fields, fields, fields, fields, P("seq", None)),
        out_specs=(fields, fields, fields, fields, P("seq", None)),
        check_vma=False,
    )
```

```python
import functools
import math

import jax
import jax.numpy as jnp
from jax import lax
from jax.sharding import PartitionSpec as P


matmul_precision = lax.Precision.HIGHEST


def dft_tables(rows, cols, total, sign):
    first = jnp.arange(rows, dtype=jnp.int32)
    second = jnp.arange(cols, dtype=jnp.int32)
    product = first[:, None] * second[None, :] % total
    angles = product.astype(jnp.float32) * (sign * 2.0 * math.pi / total)
    return (jnp.cos(angles), jnp.sin(angles))


def mix_table(size, sign):
    cosine, sine = dft_tables(size, size, size, sign)
    top = jnp.concatenate([cosine.T, sine.T], axis=1)
    bottom = jnp.concatenate([-sine.T, cosine.T], axis=1)
    return jnp.concatenate([top, bottom], axis=0)


def forward(signal, major, minor):
    padded = major * minor
    lead = signal.shape[:-1]
    held = signal.shape[-1] // minor
    blocks = signal.reshape(lead + (held, minor))
    cosine, sine = dft_tables(major, held, major, -1.0)
    part = jnp.einsum("kn,...nm->...km", jnp.concatenate([cosine, sine], axis=0), blocks, precision=matmul_precision)
    part_real, part_imag = part[..., :major, :], part[..., major:, :]
    twiddle_cos, twiddle_sin = dft_tables(major, minor, padded, -1.0)
    turned = jnp.concatenate(
        [part_real * twiddle_cos - part_imag * twiddle_sin, part_real * twiddle_sin + part_imag * twiddle_cos],
        axis=-1,
    )
    return jnp.einsum("...n,nk->...k", turned, mix_table(minor, -1.0), precision=matmul_precision)


def inverse_real(spectrum, major, minor, keep):
    padded = major * minor
    mixed = jnp.einsum("...n,nk->...k", spectrum, mix_table(minor, 1.0), precision=matmul_precision)
    mixed_real, mixed_imag = mixed[..., :minor], mixed[..., minor:]
    twiddle_cos, twiddle_sin = dft_tables(major, minor, padded, 1.0)
    turned = jnp.concatenate(
        [mixed_real * twiddle_cos - mixed_imag * twiddle_sin, mixed_real * twiddle_sin + mixed_imag * twiddle_cos],
        axis=-2,
    )
    rows = keep // minor
    cosine, sine = dft_tables(rows, major, major, 1.0)
    out = jnp.einsum("kn,...nm->...km", jnp.concatenate([cosine, -sine], axis=1), turned, precision=matmul_precision)
    return out.reshape(out.shape[:-2] + (rows * minor,))


def times(a, b, minor, conjugate_a):
    a_re, a_im = a[..., :minor], a[..., minor:]
    b_re, b_im = b[..., :minor], b[..., minor:]
    if conjugate_a:
        return jnp.concatenate([a_re * b_re + a_im * b_im, a_re * b_im - a_im * b_re], axis=-1)
    return jnp.concatenate([a_re * b_re - a_im * b_im, a_re * b_im + a_im * b_re], axis=-1)


def convolve_all(gated, grad_conv, filt):
    length = gated.shape[-1]
    padded = 2 * length
    minor = 128
    major = padded // minor
    f_spec = forward(filt, major, minor)
    spec = forward(jnp.stack([gated, grad_conv]), major, minor)
    g_spec, d_spec = spec[0], spec[1]
    pair = jnp.stack([times(f_spec, g_spec, minor, False), times(f_spec, d_spec, minor, True)])
    both = inverse_real(pair, major, minor, length) / padded
    filt_local = inverse_real(times(g_spec, d_spec, minor, True), major, minor, length) / padded
    return (both[0], both[1], filt_local)


def sum_by_doubling(part, axis):
    size = lax.axis_size(axis)
    step = 1
    while step < size:
        part = part + lax.ppermute(part, axis, [(j, j ^ step) for j in range(size)])
        step *= 2
    return part


def reduce_filter(part, dp_axes):
    if len(dp_axes) == 1:
        return lax.psum(part, dp_axes)
    wide, narrow = dp_axes
    size = lax.axis_size(narrow)
    spread = jnp.broadcast_to(part[None], (size,) + part.shape)
    got = lax.all_to_all(spread, narrow, split_axis=0, concat_axis=0, tiled=True)
    part = got[0]
    for member in range(1, size):
        part = part + got[member]
    return sum_by_doubling(part, wide)


def body(query, key_in, value, grad_out, filt, dp_axes=("dp",)):
    return body_steps(query, key_in, value, grad_out, filt, dp_axes)


def body_steps(query, key_in, value, grad_out, filt, dp_axes):
    batches = 1
    for axis in dp_axes:
        batches *= lax.axis_size(axis)
    parts = lax.axis_size("seq")
    length = filt.shape[1]
    channels = query.shape[1]
    local = query.shape[2]
    per = channels // parts
    gated = key_in[0] * value[0]
    grad_conv = grad_out[0] * query[0]
    sent = jnp.stack([gated, grad_conv]).reshape(2, parts, per, local)
    got = lax.all_to_all(sent, "seq", split_axis=1, concat_axis=1, tiled=True)
    got = jnp.swapaxes(got, 1, 2).reshape(2, per, length)
    conv, grad_gated, filt_local = convolve_all(got[0], got[1], filt)
    back = jnp.stack([conv, grad_gated]).reshape(2, per, parts, local)
    back = jnp.swapaxes(back, 1, 2)
    back = lax.all_to_all(back, "seq", split_axis=1, concat_axis=1, tiled=True)
    back = back.reshape(2, 1, channels, local)
    conv_here, gated_grad_here = back[0], back[1]
    output = query * conv_here
    grad_query = grad_out * conv_here
    grad_key = gated_grad_here * value
    grad_value = gated_grad_here * key_in
    grad_filt = reduce_filter(filt_local, dp_axes) / math.sqrt(batches * length)
    return (output, grad_query, grad_key, grad_value, grad_filt)


def solution(mesh):
    from jax.sharding import Mesh

    batches = mesh.shape["dp"]
    narrow = 3
    wide = batches // narrow
    if batches % narrow == 0 and wide & (wide - 1) == 0:
        devices = mesh.devices.reshape(wide, narrow, mesh.shape["seq"])
        mesh = Mesh(devices, ("dp_wide", "dp_narrow", "seq"))
        dp_axes = ("dp_wide", "dp_narrow")
    else:
        dp_axes = ("dp",)
    fields = P(dp_axes, None, "seq")
    return jax.shard_map(
        functools.partial(body, dp_axes=dp_axes),
        mesh=mesh,
        in_specs=(fields, fields, fields, fields, P("seq", None)),
        out_specs=(fields, fields, fields, fields, P("seq", None)),
        check_vma=False,
    )
```

```python
import functools
import math

import jax
import jax.numpy as jnp
from jax import lax
from jax.sharding import PartitionSpec as P


matmul_precision = lax.Precision.HIGHEST


def dft_tables(rows, cols, total, sign):
    first = jnp.arange(rows, dtype=jnp.int32)
    second = jnp.arange(cols, dtype=jnp.int32)
    product = first[:, None] * second[None, :] % total
    angles = product.astype(jnp.float32) * (sign * 2.0 * math.pi / total)
    return (jnp.cos(angles), jnp.sin(angles))


def mix_table(size, sign):
    cosine, sine = dft_tables(size, size, size, sign)
    top = jnp.concatenate([cosine.T, sine.T], axis=1)
    bottom = jnp.concatenate([-sine.T, cosine.T], axis=1)
    return jnp.concatenate([top, bottom], axis=0)


def forward(signal, major, minor):
    padded = major * minor
    lead = signal.shape[:-1]
    held = signal.shape[-1] // minor
    blocks = signal.reshape(lead + (held, minor))
    cosine, sine = dft_tables(major, held, major, -1.0)
    part = jnp.einsum("kn,...nm->...km", jnp.concatenate([cosine, sine], axis=0), blocks, precision=matmul_precision)
    part_real, part_imag = part[..., :major, :], part[..., major:, :]
    twiddle_cos, twiddle_sin = dft_tables(major, minor, padded, -1.0)
    turned = jnp.concatenate(
        [part_real * twiddle_cos - part_imag * twiddle_sin, part_real * twiddle_sin + part_imag * twiddle_cos],
        axis=-1,
    )
    return jnp.einsum("...n,nk->...k", turned, mix_table(minor, -1.0), precision=matmul_precision)


def inverse_real(spectrum, major, minor, keep):
    padded = major * minor
    mixed = jnp.einsum("...n,nk->...k", spectrum, mix_table(minor, 1.0), precision=matmul_precision)
    mixed_real, mixed_imag = mixed[..., :minor], mixed[..., minor:]
    twiddle_cos, twiddle_sin = dft_tables(major, minor, padded, 1.0)
    turned = jnp.concatenate(
        [mixed_real * twiddle_cos - mixed_imag * twiddle_sin, mixed_real * twiddle_sin + mixed_imag * twiddle_cos],
        axis=-2,
    )
    rows = keep // minor
    cosine, sine = dft_tables(rows, major, major, 1.0)
    out = jnp.einsum("kn,...nm->...km", jnp.concatenate([cosine, -sine], axis=1), turned, precision=matmul_precision)
    return out.reshape(out.shape[:-2] + (rows * minor,))


def times(a, b, minor, conjugate_a):
    a_re, a_im = a[..., :minor], a[..., minor:]
    b_re, b_im = b[..., :minor], b[..., minor:]
    if conjugate_a:
        return jnp.concatenate([a_re * b_re + a_im * b_im, a_re * b_im - a_im * b_re], axis=-1)
    return jnp.concatenate([a_re * b_re - a_im * b_im, a_re * b_im + a_im * b_re], axis=-1)


def convolve_all(gated, grad_conv, filt):
    length = gated.shape[-1]
    padded = 2 * length
    minor = 128
    major = padded // minor
    f_spec = forward(filt, major, minor)
    spec = forward(jnp.stack([gated, grad_conv]), major, minor)
    g_spec, d_spec = spec[0], spec[1]
    pair = jnp.stack([times(f_spec, g_spec, minor, False), times(f_spec, d_spec, minor, True)])
    both = inverse_real(pair, major, minor, length) / padded
    filt_local = inverse_real(times(g_spec, d_spec, minor, True), major, minor, length) / padded
    return (both[0], both[1], filt_local)


def sum_in_order(part, axis):
    size = lax.axis_size(axis)
    me = lax.axis_index(axis)
    held = {0: part}
    for shift in range(size - 1, 0, -1):
        held[shift] = lax.ppermute(part, axis, [(j, (j + shift) % size) for j in range(size)])
    total = None
    for member in range(size):
        value = held[0]
        for shift in range(1, size):
            value = jnp.where((me - shift) % size == member, held[shift], value)
        total = value if total is None else total + value
    return total


def sum_by_doubling(part, axis):
    size = lax.axis_size(axis)
    step = size // 2
    while step >= 1:
        part = part + lax.ppermute(part, axis, [(j, j ^ step) for j in range(size)])
        step //= 2
    return part


def reduce_filter(part, dp_axes):
    if len(dp_axes) == 1:
        return lax.psum(part, dp_axes)
    wide, narrow = dp_axes
    part = sum_in_order(part, narrow)
    return sum_by_doubling(part, wide)


def body(query, key_in, value, grad_out, filt, dp_axes=("dp",)):
    return body_steps(query, key_in, value, grad_out, filt, dp_axes)


def body_steps(query, key_in, value, grad_out, filt, dp_axes):
    batches = 1
    for axis in dp_axes:
        batches *= lax.axis_size(axis)
    parts = lax.axis_size("seq")
    length = filt.shape[1]
    channels = query.shape[1]
    local = query.shape[2]
    per = channels // parts
    gated = key_in[0] * value[0]
    grad_conv = grad_out[0] * query[0]
    sent = jnp.stack([gated, grad_conv]).reshape(2, parts, per, local)
    got = lax.all_to_all(sent, "seq", split_axis=1, concat_axis=1, tiled=True)
    got = jnp.swapaxes(got, 1, 2).reshape(2, per, length)
    conv, grad_gated, filt_local = convolve_all(got[0], got[1], filt)
    back = jnp.stack([conv, grad_gated]).reshape(2, per, parts, local)
    back = jnp.swapaxes(back, 1, 2)
    back = lax.all_to_all(back, "seq", split_axis=1, concat_axis=1, tiled=True)
    back = back.reshape(2, 1, channels, local)
    conv_here, gated_grad_here = back[0], back[1]
    output = query * conv_here
    grad_query = grad_out * conv_here
    grad_key = gated_grad_here * value
    grad_value = gated_grad_here * key_in
    grad_filt = reduce_filter(filt_local, dp_axes) / math.sqrt(batches * length)
    return (output, grad_query, grad_key, grad_value, grad_filt)


def solution(mesh):
    from jax.sharding import Mesh

    batches = mesh.shape["dp"]
    narrow = 3
    wide = batches // narrow
    if batches % narrow == 0 and wide & (wide - 1) == 0:
        devices = mesh.devices.reshape(wide, narrow, mesh.shape["seq"])
        mesh = Mesh(devices, ("dp_wide", "dp_narrow", "seq"))
        dp_axes = ("dp_wide", "dp_narrow")
    else:
        dp_axes = ("dp",)
    fields = P(dp_axes, None, "seq")
    return jax.shard_map(
        functools.partial(body, dp_axes=dp_axes),
        mesh=mesh,
        in_specs=(fields, fields, fields, fields, P("seq", None)),
        out_specs=(fields, fields, fields, fields, P("seq", None)),
        check_vma=False,
    )
```

```python
import functools
import math

import jax
import jax.numpy as jnp
from jax import lax
from jax.sharding import PartitionSpec as P


matmul_precision = lax.Precision.HIGHEST


def dft_tables(rows, cols, total, sign):
    first = jnp.arange(rows, dtype=jnp.int32)
    second = jnp.arange(cols, dtype=jnp.int32)
    product = first[:, None] * second[None, :] % total
    angles = product.astype(jnp.float32) * (sign * 2.0 * math.pi / total)
    return (jnp.cos(angles), jnp.sin(angles))


def mix_table(size, sign):
    cosine, sine = dft_tables(size, size, size, sign)
    top = jnp.concatenate([cosine.T, sine.T], axis=1)
    bottom = jnp.concatenate([-sine.T, cosine.T], axis=1)
    return jnp.concatenate([top, bottom], axis=0)


def forward(signal, major, minor):
    padded = major * minor
    lead = signal.shape[:-1]
    held = signal.shape[-1] // minor
    blocks = signal.reshape(lead + (held, minor))
    cosine, sine = dft_tables(major, held, major, -1.0)
    part = jnp.einsum("kn,...nm->...km", jnp.concatenate([cosine, sine], axis=0), blocks, precision=matmul_precision)
    part_real, part_imag = part[..., :major, :], part[..., major:, :]
    twiddle_cos, twiddle_sin = dft_tables(major, minor, padded, -1.0)
    turned = jnp.concatenate(
        [part_real * twiddle_cos - part_imag * twiddle_sin, part_real * twiddle_sin + part_imag * twiddle_cos],
        axis=-1,
    )
    return jnp.einsum("...n,nk->...k", turned, mix_table(minor, -1.0), precision=matmul_precision)


def inverse_real(spectrum, major, minor, keep):
    padded = major * minor
    mixed = jnp.einsum("...n,nk->...k", spectrum, mix_table(minor, 1.0), precision=matmul_precision)
    mixed_real, mixed_imag = mixed[..., :minor], mixed[..., minor:]
    twiddle_cos, twiddle_sin = dft_tables(major, minor, padded, 1.0)
    turned = jnp.concatenate(
        [mixed_real * twiddle_cos - mixed_imag * twiddle_sin, mixed_real * twiddle_sin + mixed_imag * twiddle_cos],
        axis=-2,
    )
    rows = keep // minor
    cosine, sine = dft_tables(rows, major, major, 1.0)
    out = jnp.einsum("kn,...nm->...km", jnp.concatenate([cosine, -sine], axis=1), turned, precision=matmul_precision)
    return out.reshape(out.shape[:-2] + (rows * minor,))


def times(a, b, minor, conjugate_a):
    a_re, a_im = a[..., :minor], a[..., minor:]
    b_re, b_im = b[..., :minor], b[..., minor:]
    if conjugate_a:
        return jnp.concatenate([a_re * b_re + a_im * b_im, a_re * b_im - a_im * b_re], axis=-1)
    return jnp.concatenate([a_re * b_re - a_im * b_im, a_re * b_im + a_im * b_re], axis=-1)


def convolve_all(gated, grad_conv, filt):
    length = gated.shape[-1]
    padded = 2 * length
    minor = 128
    major = padded // minor
    f_spec = forward(filt, major, minor)
    spec = forward(jnp.stack([gated, grad_conv]), major, minor)
    g_spec, d_spec = spec[0], spec[1]
    pair = jnp.stack([times(f_spec, g_spec, minor, False), times(f_spec, d_spec, minor, True)])
    both = inverse_real(pair, major, minor, length) / padded
    filt_local = inverse_real(times(g_spec, d_spec, minor, True), major, minor, length) / padded
    return (both[0], both[1], filt_local)


def sum_in_order(part, axis):
    size = lax.axis_size(axis)
    me = lax.axis_index(axis)
    held = {0: part}
    for shift in range(1, size):
        held[shift] = lax.ppermute(part, axis, [(j, (j + shift) % size) for j in range(size)])
    total = None
    for member in range(size):
        value = held[0]
        for shift in range(1, size):
            value = jnp.where((me - shift) % size == member, held[shift], value)
        total = value if total is None else total + value
    return total


def sum_by_doubling(part, axis):
    size = lax.axis_size(axis)
    step = size // 2
    while step >= 1:
        part = part + lax.ppermute(part, axis, [(j, j ^ step) for j in range(size)])
        step //= 2
    return part


def reduce_filter(part, dp_axes):
    if len(dp_axes) == 1:
        return lax.psum(part, dp_axes)
    wide, narrow = dp_axes
    part = sum_in_order(part, narrow)
    return sum_by_doubling(part, wide)


def body(query, key_in, value, grad_out, filt, dp_axes=("dp",)):
    return body_steps(query, key_in, value, grad_out, filt, dp_axes)


def body_steps(query, key_in, value, grad_out, filt, dp_axes):
    batches = 1
    for axis in dp_axes:
        batches *= lax.axis_size(axis)
    parts = lax.axis_size("seq")
    length = filt.shape[1]
    channels = query.shape[1]
    local = query.shape[2]
    per = channels // parts
    sent = (jnp.stack([key_in[0], grad_out[0]]) * jnp.stack([value[0], query[0]])).reshape(2, parts, per, local)
    got = lax.all_to_all(sent, "seq", split_axis=1, concat_axis=1, tiled=True)
    got = jnp.swapaxes(got, 1, 2).reshape(2, per, length)
    conv, grad_gated, filt_local = convolve_all(got[0], got[1], filt)
    back = jnp.stack([conv, grad_gated]).reshape(2, per, parts, local)
    back = jnp.swapaxes(back, 1, 2)
    back = lax.all_to_all(back, "seq", split_axis=1, concat_axis=1, tiled=True)
    back = back.reshape(2, 1, channels, local)
    conv_here, gated_grad_here = back[0], back[1]
    output = query * conv_here
    grad_query = grad_out * conv_here
    grad_key = gated_grad_here * value
    grad_value = gated_grad_here * key_in
    grad_filt = reduce_filter(filt_local, dp_axes) / math.sqrt(batches * length)
    return (output, grad_query, grad_key, grad_value, grad_filt)


def solution(mesh):
    from jax.sharding import Mesh

    batches = mesh.shape["dp"]
    narrow = 3
    wide = batches // narrow
    if batches % narrow == 0 and wide & (wide - 1) == 0:
        devices = mesh.devices.reshape(wide, narrow, mesh.shape["seq"])
        mesh = Mesh(devices, ("dp_wide", "dp_narrow", "seq"))
        dp_axes = ("dp_wide", "dp_narrow")
    else:
        dp_axes = ("dp",)
    fields = P(dp_axes, None, "seq")
    return jax.shard_map(
        functools.partial(body, dp_axes=dp_axes),
        mesh=mesh,
        in_specs=(fields, fields, fields, fields, P("seq", None)),
        out_specs=(fields, fields, fields, fields, P("seq", None)),
        check_vma=False,
    )
```
